256 devices in a mesh: dp: 32 (over y, x, core), tensor: 8 (over z).
Axes of the slice: x: 4, y: 4, z: 8, core: 2. Of those that a mesh axis runs over, the one named last changes fastest.
Arguments:
- tokens: bfloat16 [8192, 8192], P('dp'), may hold values from -6 to 6
- router_weight: bfloat16 [8192, 32], replicated, may hold values from -0.0625 to 0.0625
- gate_weight: bfloat16 [14336, 8192], P(('dp', 'tensor')), may hold values from -0.0625 to 0.0625
- up_weight: bfloat16 [14336, 8192], P(('dp', 'tensor')), may hold values from -0.0625 to 0.0625
- down_weight: bfloat16 [14336, 8192], P(('dp', 'tensor')), may hold values from -0.25 to 0.25
- cluster_of: int32 [14336, 1], P('dp'), may hold values from 0 to 31; in each aligned block of 448 rows (0 to 447, 448 to 895, ...) at most 28 rows name the same one
- expert_ids: int32 [8192, 2], P('dp'), may hold values from 0 to 31, all different within a row; in each aligned block of 256 rows (0 to 255, 256 to 511, ...) at most 32 rows name the same one
Outputs:
- mixed_out: bfloat16 [8192, 8192], P('dp', 'tensor')
The draws below stay inside these ranges and needn't reach their ends.
Inputs may be any that keep to these rules, and one draw needn't show every extreme that they name: `expert_ids`: in each aligned block of 256 rows (the tokens of one dp index) no expert is named by more than 32 rows, a bound that some block reaches; a row names two different experts; every expert is named somewhere. `cluster_of`: in each aligned block of 448 hidden units no cluster holds more than 28 units, and some cluster holds exactly 28; every cluster holds some unit.
All inputs are finite; a program needn't handle non-finite values.
Results may differ from the reference program's by a relative error of at most 0.023.
Values may be sent and summed in bfloat16 or wider, within the bound.
No kernel may reach another device: no remote copies, remote signals or barrier semaphores. Data moves between devices by JAX's collectives and lax.ppermute only.
A program may use at most 64 MiB of HBM per device.

```python
import math
import jax
import jax.numpy as jnp
import numpy as np
from jax import lax

D = 8192
FF = 14336
TOK_DP = 256
EXPERTS = 32
CAP = 32
UCAP = 28
TOKENS = 8192
N_DP = 32
N_TENSOR = 8


def levels(rng, extent, cuts, smallest, top_value):
    factor_of, own = 1.0, jax.random.fold_in(rng, 6)
    for dim, blocks in cuts:
        steps = jnp.exp(jax.random.uniform(jax.random.fold_in(own, dim), (blocks,), jnp.float32, smallest / len(cuts), top_value / len(cuts)))
        factor_of = factor_of * jnp.repeat(steps, extent[dim] // blocks).reshape([-1 if axis == dim else 1 for axis in range(len(extent))])
    return factor_of


def shared_out(key, own, number, rows, count, top, reach, skew):
    ranking = jax.random.permutation(key, count)
    heavy_load, common = load_shares(count, rows * top, reach, skew, True), load_shares(count, rows * top, reach, skew, False)
    places = jnp.arange(count)

    def named(lengths, offset_by):
        used = int((lengths > 0).sum())
        fixed = max(1, used // 4)
        shifted = fixed + (places - fixed + offset_by * (used - fixed)) % max(1, count - fixed)
        return jnp.zeros((count,), jnp.int32).at[ranking[jnp.where(places < fixed, places, shifted)]].set(jnp.asarray(lengths, jnp.int32))

    lengths = jnp.where(number % 4 == 0, named(heavy_load, number // 4), named(common, number - number // 4 - 1))
    mixed = jax.random.permutation(jax.random.fold_in(own, 3), count)
    source_of, sink = mixed[0:count // 2 * 2:2], mixed[1:count // 2 * 2:2]
    margin = jnp.minimum(lengths[source_of] - 1, reach - lengths[sink]) // 2
    margin = jnp.where((source_of == ranking[0]) | (sink == ranking[0]) | (lengths[sink] == 0), 0, jnp.maximum(margin, 0))
    shifted = jax.random.randint(jax.random.fold_in(own, 4), (count // 2,), 0, 1 << 20) % (margin + 1)
    lengths = lengths.at[source_of].add(-shifted).at[sink].add(shifted)
    labels = jnp.searchsorted(jnp.cumsum(lengths), jnp.arange(rows * top), side="right").astype(jnp.int32)
    grid = labels.reshape(top, rows).T
    grid = grid[jax.random.permutation(jax.random.fold_in(own, 1), rows)]
    offset_by = jax.random.randint(jax.random.fold_in(own, 2), (rows, 1), 0, top)
    return jnp.take_along_axis(grid, (jnp.arange(top)[None, :] + offset_by) % top, axis=1)


def load_shares(number_of, total, bound, slope, full):
    portions = [(1 << 20) // math.isqrt(standing ** slope) + 1 for standing in range(1, number_of + 1)]
    largest = bound if full else min(bound, max(-(-total // number_of), total * portions[0] // sum(portions)))
    least = 1 if total - largest >= number_of - 1 else 0
    counts, surplus = [largest] + [least] * (number_of - 1), total - largest - least * (number_of - 1)
    while surplus > 0:
        free = [i for i in range(1, number_of) if counts[i] < largest] or [i for i in range(1, number_of) if counts[i] < bound]
        mass, budget = sum([portions[i] for i in free]), surplus
        for i in free:
            extra = min(bound - counts[i], max(1, budget * portions[i] // mass), surplus)
            counts[i] = counts[i] + extra
            surplus = surplus - extra
    return np.array(counts)


def gaussian(key, dims, deviation, bound, cuts=(), dtype=jnp.bfloat16):
    values = jax.random.normal(key, dims, jnp.float32) * deviation
    if len(cuts) > 0:
        values = levels(key, dims, cuts, -0.22, 0.18) * values
    return jnp.clip(values, min=-bound, max=bound).astype(dtype)


def setup_inputs(seed: int = 0) -> dict:
    streams_of = jax.random.split(jax.random.key(seed), 8)
    tokens = gaussian(streams_of[0], (TOKENS, D), 1.0, 6.0, ((0, 32),))
    router_weight = gaussian(streams_of[1], (D, EXPERTS), D ** -0.5, 0.0625)
    gate_weight = gaussian(streams_of[2], (FF, D), D ** -0.5, 0.0625, ((0, 256),))
    up_weight = gaussian(streams_of[3], (FF, D), D ** -0.5, 0.0625, ((0, 256),))
    down_weight = gaussian(streams_of[4], (FF, D), (FF // EXPERTS) ** -0.5, 0.25, ((0, 256),))
    cluster_of_keys = jax.random.split(jax.random.fold_in(streams_of[5], 1), FF // (FF // N_DP))
    cluster_of_turns = jax.random.permutation(jax.random.fold_in(streams_of[5], 3), FF // (FF // N_DP))
    cluster_of = jax.vmap(lambda own, number: shared_out(jax.random.fold_in(streams_of[5], 2), own, number, FF // N_DP, EXPERTS, 1, UCAP, 1))(cluster_of_keys, cluster_of_turns).reshape((FF, 1))
    expert_ids_keys = jax.random.split(jax.random.fold_in(streams_of[6], 1), TOKENS // TOK_DP)
    expert_ids_turns = jax.random.permutation(jax.random.fold_in(streams_of[6], 3), TOKENS // TOK_DP)
    expert_ids = jax.vmap(lambda own, number: shared_out(jax.random.fold_in(streams_of[6], 2), own, number, TOK_DP, EXPERTS, 2, CAP, 2))(expert_ids_keys, expert_ids_turns).reshape((TOKENS, 2))
    return {"tokens": tokens, "router_weight": router_weight, "gate_weight": gate_weight, "up_weight": up_weight, "down_weight": down_weight, "cluster_of": cluster_of, "expert_ids": expert_ids}


def against(left_side, right_side):
    return lax.dot_general(left_side, right_side, (((1,), (1,)), ((), ())), preferred_element_type=jnp.float32)


def reference(tokens, router_weight, gate_weight, up_weight, down_weight, cluster_of, expert_ids):
    width_part = D // N_TENSOR
    logits = jnp.dot(tokens, router_weight, preferred_element_type=jnp.float32)
    scores = jax.nn.sigmoid(jnp.take_along_axis(logits, expert_ids, axis=1))
    mixing = scores / jnp.sum(scores, axis=1, keepdims=True)
    unit_cluster = cluster_of[:, 0]
    block_rows = 512 if TOKENS % 512 == 0 else TOKENS
    count_blocks = TOKENS // block_rows

    def one_block(inputs):
        token_block, id_block, mix_block = inputs
        gate_sum = jnp.zeros((block_rows, FF), jnp.float32)
        up_sum = jnp.zeros((block_rows, FF), jnp.float32)
        for block_index in range(N_TENSOR):
            lower = block_index * width_part
            piece = token_block[:, lower:lower + width_part]
            gate_term = against(piece, gate_weight[:, lower:lower + width_part]).astype(jnp.bfloat16)
            up_term = against(piece, up_weight[:, lower:lower + width_part]).astype(jnp.bfloat16)
            gate_sum = gate_sum + lax.optimization_barrier(gate_term).astype(jnp.float32)
            up_sum = up_sum + lax.optimization_barrier(up_term).astype(jnp.float32)
        hidden = (jax.nn.silu(gate_sum) * up_sum).astype(jnp.bfloat16)
        total = jnp.zeros((block_rows, D), jnp.float32)
        for slot_index in range(2):
            keep = unit_cluster[None, :] == id_block[:, slot_index:slot_index + 1]
            masked = jnp.where(keep, hidden, jnp.zeros_like(hidden))
            expert_out = jnp.dot(masked, down_weight, preferred_element_type=jnp.float32).astype(jnp.bfloat16)
            total = total + mix_block[:, slot_index:slot_index + 1] * lax.optimization_barrier(expert_out).astype(jnp.float32)
        return total.astype(jnp.bfloat16)

    outputs = lax.map(one_block, (tokens.reshape(count_blocks, block_rows, D),
                                  expert_ids.reshape(count_blocks, block_rows, 2),
                                  mixing.reshape(count_blocks, block_rows, 2)))
    return outputs.reshape(TOKENS, D)
```

```python
import jax
import jax.numpy as jnp
from jax import lax
from jax.sharding import PartitionSpec as P


def place_rows(labels, bin_count, capacity):
    count_rows = labels.shape[0]
    onehot = (labels[:, None] == jnp.arange(bin_count, dtype=jnp.int32)[None, :]).astype(jnp.int32)
    before = jnp.cumsum(onehot, axis=0) - onehot
    rank_in = jnp.sum(before * onehot, axis=1)
    position = labels * capacity + rank_in
    slot_list = jnp.full((bin_count * capacity,), count_rows, jnp.int32)
    slot_list = slot_list.at[position].set(jnp.arange(count_rows, dtype=jnp.int32))
    return (slot_list, position)


def with_zero_row(matrix):
    pad = jnp.zeros((1,) + matrix.shape[1:], matrix.dtype)
    return jnp.concatenate([matrix, pad], axis=0)


def against(left_side, right_side):
    return lax.dot_general(
        left_side, right_side, (((1,), (1,)), ((), ())), preferred_element_type=jnp.float32
    )


def on_device(tokens, router_weight, gate_weight, up_weight, down_weight, cluster_of, expert_ids):
    owners = lax.axis_size("dp")
    tensor_count = lax.axis_size("tensor")
    width_part = tokens.shape[1] // tensor_count
    token_count = tokens.shape[0]

    logits = jnp.dot(tokens, router_weight, preferred_element_type=jnp.float32)
    scores = jax.nn.sigmoid(jnp.take_along_axis(logits, expert_ids, axis=1))
    mixing = scores / jnp.sum(scores, axis=1, keepdims=True)

    stacked = jnp.stack([gate_weight, up_weight, down_weight], axis=1)
    rows = lax.all_to_all(stacked, "tensor", split_axis=2, concat_axis=0, tiled=True)
    unit_cap = 2 * rows.shape[0] // owners
    unit_list, unit_spot = place_rows(cluster_of[:, 0], owners, unit_cap)
    pick = with_zero_row(rows)[unit_list]
    own = lax.all_to_all(pick, "dp", split_axis=0, concat_axis=0, tiled=True)

    capacity = 4 * token_count // owners
    flat_ids = expert_ids.reshape(-1)
    slot_list, slot_spot = place_rows(flat_ids, owners, capacity)
    features = lax.dynamic_slice_in_dim(
        tokens, lax.axis_index("tensor") * width_part, width_part, 1
    )
    outgoing = with_zero_row(features)[slot_list // 2]
    arrived = lax.all_to_all(outgoing, "dp", split_axis=0, concat_axis=0, tiled=True)

    gate_part = against(arrived, own[:, 0, :]).astype(jnp.bfloat16)
    up_part = against(arrived, own[:, 1, :]).astype(jnp.bfloat16)
    both = jnp.stack([gate_part, up_part], axis=1)
    summed = lax.psum_scatter(both, "tensor", scatter_dimension=0, tiled=True).astype(jnp.float32)
    hidden_part = (jax.nn.silu(summed[:, 0, :]) * summed[:, 1, :]).astype(jnp.bfloat16)
    hidden = lax.all_gather(hidden_part, "tensor", axis=0, tiled=True)
    expert_out = jnp.dot(hidden, own[:, 2, :], preferred_element_type=jnp.float32).astype(jnp.bfloat16)
    returned = lax.all_to_all(expert_out, "dp", split_axis=0, concat_axis=0, tiled=True)
    picked_out = returned[slot_spot].reshape(token_count, 2, width_part)
    mixed_out = jnp.sum(mixing[:, :, None] * picked_out.astype(jnp.float32), axis=1)
    return mixed_out.astype(jnp.bfloat16)


def solution(mesh):
    in_specs = (
        P("dp", None),
        P(),
        P(("dp", "tensor"), None),
        P(("dp", "tensor"), None),
        P(("dp", "tensor"), None),
        P("dp", None),
        P("dp", None),
    )
    out_specs = P("dp", "tensor")
    return jax.shard_map(
        on_device, mesh=mesh, in_specs=in_specs, out_specs=out_specs, check_vma=False
    )
```

```python
import jax
import jax.numpy as jnp
from jax import lax
from jax.sharding import PartitionSpec as P


def place_rows(labels, bin_count, capacity):
    count_rows = labels.shape[0]
    onehot = (labels[:, None] == jnp.arange(bin_count, dtype=jnp.int32)[None, :]).astype(jnp.int32)
    before = jnp.cumsum(onehot, axis=0) - onehot
    rank_in = jnp.sum(before * onehot, axis=1)
    position = labels * capacity + rank_in
    slot_list = jnp.full((bin_count * capacity,), count_rows, jnp.int32)
    slot_list = slot_list.at[position].set(jnp.arange(count_rows, dtype=jnp.int32))
    return (slot_list, position)


def against(left_side, right_side):
    return lax.dot_general(
        left_side, right_side, (((1,), (1,)), ((), ())), preferred_element_type=jnp.float32
    )


def select_rows(index, table):
    hot = (index[:, None] == jnp.arange(table.shape[0], dtype=jnp.int32)[None, :]).astype(table.dtype)
    return jnp.dot(hot, table, preferred_element_type=jnp.float32).astype(table.dtype)


def exchange_features(weights, tensor_count):
    me = lax.axis_index("tensor")
    lead = weights.shape[:-1]
    width = weights.shape[-1] // tensor_count
    blocks = weights.reshape(lead + (tensor_count, width))
    pieces = []
    for k in range(tensor_count):
        piece = lax.dynamic_index_in_dim(blocks, (me + k) % tensor_count, axis=len(lead), keepdims=False)
        if k:
            pairs = [(i, (i + k) % tensor_count) for i in range(tensor_count)]
            piece = lax.ppermute(piece, "tensor", pairs)
        pieces.append(piece)
    return jnp.concatenate(pieces, axis=len(lead) - 1)


def on_device(tokens, router_weight, gate_weight, up_weight, down_weight, cluster_of, expert_ids):
    owners = lax.axis_size("dp")
    tensor_count = lax.axis_size("tensor")
    width_part = tokens.shape[1] // tensor_count
    token_count = tokens.shape[0]
    me = lax.axis_index("tensor")

    logits = jnp.dot(tokens, router_weight, preferred_element_type=jnp.float32)
    scores = jax.nn.sigmoid(jnp.take_along_axis(logits, expert_ids, axis=1))
    mixing = scores / jnp.sum(scores, axis=1, keepdims=True)

    capacity = 4 * token_count // owners
    flat_ids = expert_ids.reshape(-1)
    slot_list, slot_spot = place_rows(flat_ids, owners, capacity)
    features = lax.dynamic_slice_in_dim(tokens, me * width_part, width_part, 1)
    outgoing = select_rows(slot_list // 2, features)
    arrived = lax.all_to_all(outgoing, "dp", split_axis=0, concat_axis=0, tiled=True)

    slice_rows = gate_weight.shape[0]
    block_rows = slice_rows * tensor_count
    unit_cap = 2 * block_rows // owners
    unit_list, _ = place_rows(cluster_of[:, 0], owners, unit_cap)
    source = unit_list // slice_rows
    local = ((me - source) % tensor_count) * slice_rows + unit_list % slice_rows
    local = jnp.where(unit_list < block_rows, local, block_rows)

    gate_up = exchange_features(jnp.stack([gate_weight, up_weight]), tensor_count)
    gate_own = lax.all_to_all(select_rows(local, gate_up[0]), "dp", split_axis=0, concat_axis=0, tiled=True)
    up_own = lax.all_to_all(select_rows(local, gate_up[1]), "dp", split_axis=0, concat_axis=0, tiled=True)
    down_rows = exchange_features(down_weight, tensor_count)
    down_own = lax.all_to_all(select_rows(local, down_rows), "dp", split_axis=0, concat_axis=0, tiled=True)

    gate_part = against(arrived, gate_own).astype(jnp.bfloat16)
    up_part = against(arrived, up_own).astype(jnp.bfloat16)
    both = jnp.stack([gate_part, up_part], axis=1)
    summed = lax.psum_scatter(both, "tensor", scatter_dimension=0, tiled=True).astype(jnp.float32)
    hidden_part = (jax.nn.silu(summed[:, 0, :]) * summed[:, 1, :]).astype(jnp.bfloat16)
    hidden = lax.all_gather(hidden_part, "tensor", axis=0, tiled=True)
    expert_out = jnp.dot(hidden, down_own, preferred_element_type=jnp.float32).astype(jnp.bfloat16)
    returned = lax.all_to_all(expert_out, "dp", split_axis=0, concat_axis=0, tiled=True)

    spots = slot_spot.reshape(token_count, 2)
    columns = jnp.arange(returned.shape[0], dtype=jnp.int32)[None, :]
    weighting = (
        jnp.where(spots[:, 0:1] == columns, mixing[:, 0:1], 0.0)
        + jnp.where(spots[:, 1:2] == columns, mixing[:, 1:2], 0.0)
    )
    mixed_out = jnp.dot(
        weighting, returned.astype(jnp.float32), precision=lax.Precision.HIGHEST,
        preferred_element_type=jnp.float32,
    )
    return mixed_out.astype(jnp.bfloat16)


def solution(mesh):
    in_specs = (
        P("dp", None),
        P(),
        P(("dp", "tensor"), None),
        P(("dp", "tensor"), None),
        P(("dp", "tensor"), None),
        P("dp", None),
        P("dp", None),
    )
    out_specs = P("dp", "tensor")
    return jax.shard_map(
        on_device, mesh=mesh, in_specs=in_specs, out_specs=out_specs, check_vma=False
    )
```

```python
import jax
import jax.numpy as jnp
from jax import lax
from jax.sharding import PartitionSpec as P


def place_rows(labels, bin_count, capacity):
    count_rows = labels.shape[0]
    onehot = (labels[:, None] == jnp.arange(bin_count, dtype=jnp.int32)[None, :]).astype(jnp.int32)
    before = jnp.cumsum(onehot, axis=0) - onehot
    rank_in = jnp.sum(before * onehot, axis=1)
    position = labels * capacity + rank_in
    slot_list = jnp.full((bin_count * capacity,), count_rows, jnp.int32)
    slot_list = slot_list.at[position].set(jnp.arange(count_rows, dtype=jnp.int32))
    return (slot_list, position)


def against(left_side, right_side):
    return lax.dot_general(
        left_side, right_side, (((1,), (1,)), ((), ())), preferred_element_type=jnp.float32
    )


def select_rows(index, table):
    hot = (index[:, None] == jnp.arange(table.shape[0], dtype=jnp.int32)[None, :]).astype(table.dtype)
    return jnp.dot(hot, table, preferred_element_type=jnp.float32).astype(table.dtype)


def exchange_features(weights, tensor_count):
    me = lax.axis_index("tensor")
    lead = weights.shape[:-1]
    width = weights.shape[-1] // tensor_count
    blocks = weights.reshape(lead + (tensor_count, width))
    pieces = []
    for k in range(tensor_count):
        piece = lax.dynamic_index_in_dim(blocks, (me + k) % tensor_count, axis=len(lead), keepdims=False)
        if k:
            pairs = [(i, (i + k) % tensor_count) for i in range(tensor_count)]
            piece = lax.ppermute(piece, "tensor", pairs)
        pieces.append(piece)
    return jnp.concatenate(pieces, axis=len(lead) - 1)


def on_device(tokens, router_weight, gate_weight, up_weight, down_weight, cluster_of, expert_ids):
    owners = lax.axis_size("dp")
    tensor_count = lax.axis_size("tensor")
    width_part = tokens.shape[1] // tensor_count
    token_count = tokens.shape[0]
    me = lax.axis_index("tensor")

    logits = jnp.dot(tokens, router_weight, preferred_element_type=jnp.float32)
    scores = jax.nn.sigmoid(jnp.take_along_axis(logits, expert_ids, axis=1))
    mixing = scores / jnp.sum(scores, axis=1, keepdims=True)

    capacity = 4 * token_count // owners
    flat_ids = expert_ids.reshape(-1)
    slot_list, slot_spot = place_rows(flat_ids, owners, capacity)
    features = lax.dynamic_slice_in_dim(tokens, me * width_part, width_part, 1)
    outgoing = select_rows(slot_list // 2, features)
    arrived = lax.all_to_all(outgoing, "dp", split_axis=0, concat_axis=0, tiled=True)

    slice_rows = gate_weight.shape[0]
    block_rows = slice_rows * tensor_count
    unit_cap = 2 * block_rows // owners
    unit_list, _ = place_rows(cluster_of[:, 0], owners, unit_cap)
    source = unit_list // slice_rows
    local = ((me - source) % tensor_count) * slice_rows + unit_list % slice_rows
    local = jnp.where(unit_list < block_rows, local, block_rows)

    gate_up = exchange_features(jnp.stack([gate_weight, up_weight]), tensor_count)
    gate_own = lax.all_to_all(select_rows(local, gate_up[0]), "dp", split_axis=0, concat_axis=0, tiled=True)
    up_own = lax.all_to_all(select_rows(local, gate_up[1]), "dp", split_axis=0, concat_axis=0, tiled=True)
    down_rows = exchange_features(down_weight, tensor_count)

    gate_part = against(arrived, gate_own).astype(jnp.bfloat16)
    gate_sum = lax.psum_scatter(gate_part, "tensor", scatter_dimension=0, tiled=True)
    gate_sum, up_own, down_rows = lax.optimization_barrier((gate_sum, up_own, down_rows))
    up_part = against(arrived, up_own).astype(jnp.bfloat16)
    down_own = lax.all_to_all(select_rows(local, down_rows), "dp", split_axis=0, concat_axis=0, tiled=True)
    up_sum = lax.psum_scatter(up_part, "tensor", scatter_dimension=0, tiled=True)
    gate_sum = gate_sum.astype(jnp.float32)
    hidden_part = (jax.nn.silu(gate_sum) * up_sum.astype(jnp.float32)).astype(jnp.bfloat16)
    hidden = lax.all_gather(hidden_part, "tensor", axis=0, tiled=True)
    expert_out = jnp.dot(hidden, down_own, preferred_element_type=jnp.float32).astype(jnp.bfloat16)
    returned = lax.all_to_all(expert_out, "dp", split_axis=0, concat_axis=0, tiled=True)

    spots = slot_spot.reshape(token_count, 2)
    columns = jnp.arange(returned.shape[0], dtype=jnp.int32)[None, :]
    weighting = (
        jnp.where(spots[:, 0:1] == columns, mixing[:, 0:1], 0.0)
        + jnp.where(spots[:, 1:2] == columns, mixing[:, 1:2], 0.0)
    )
    mixed_out = jnp.dot(
        weighting, returned.astype(jnp.float32), precision=lax.Precision.HIGHEST,
        preferred_element_type=jnp.float32,
    )
    return mixed_out.astype(jnp.bfloat16)


def solution(mesh):
    in_specs = (
        P("dp", None),
        P(),
        P(("dp", "tensor"), None),
        P(("dp", "tensor"), None),
        P(("dp", "tensor"), None),
        P("dp", None),
        P("dp", None),
    )
    out_specs = P("dp", "tensor")
    return jax.shard_map(
        on_device, mesh=mesh, in_specs=in_specs, out_specs=out_specs, check_vma=False
    )
```

```python
import jax
import jax.numpy as jnp
from jax import lax
from jax.sharding import PartitionSpec as P


def place_rows(labels, bin_count, capacity):
    count_rows = labels.shape[0]
    onehot = (labels[:, None] == jnp.arange(bin_count, dtype=jnp.int32)[None, :]).astype(jnp.int32)
    before = jnp.cumsum(onehot, axis=0) - onehot
    rank_in = jnp.sum(before * onehot, axis=1)
    position = labels * capacity + rank_in
    slot_list = jnp.full((bin_count * capacity,), count_rows, jnp.int32)
    slot_list = slot_list.at[position].set(jnp.arange(count_rows, dtype=jnp.int32))
    return (slot_list, position)


def against(left_side, right_side):
    return lax.dot_general(
        left_side, right_side, (((1,), (1,)), ((), ())), preferred_element_type=jnp.float32
    )


def select_rows(index, table):
    hot = (index[:, None] == jnp.arange(table.shape[0], dtype=jnp.int32)[None, :]).astype(table.dtype)
    return jnp.dot(hot, table, preferred_element_type=jnp.float32).astype(table.dtype)


def exchange_features(weights, tensor_count):
    me = lax.axis_index("tensor")
    lead = weights.shape[:-1]
    width = weights.shape[-1] // tensor_count
    blocks = weights.reshape(lead + (tensor_count, width))
    pieces = []
    for k in range(tensor_count):
        piece = lax.dynamic_index_in_dim(blocks, (me + k) % tensor_count, axis=len(lead), keepdims=False)
        if k:
            pairs = [(i, (i + k) % tensor_count) for i in range(tensor_count)]
            piece = lax.ppermute(piece, "tensor", pairs)
        pieces.append(piece)
    return jnp.concatenate(pieces, axis=len(lead) - 1)


def on_device(tokens, router_weight, gate_weight, up_weight, down_weight, cluster_of, expert_ids):
    owners = lax.axis_size("dp")
    tensor_count = lax.axis_size("tensor")
    width_part = tokens.shape[1] // tensor_count
    token_count = tokens.shape[0]
    me = lax.axis_index("tensor")

    logits = jnp.dot(tokens, router_weight, preferred_element_type=jnp.float32)
    scores = jax.nn.sigmoid(jnp.take_along_axis(logits, expert_ids, axis=1))
    mixing = scores / jnp.sum(scores, axis=1, keepdims=True)

    capacity = 4 * token_count // owners
    flat_ids = expert_ids.reshape(-1)
    slot_list, slot_spot = place_rows(flat_ids, owners, capacity)
    features = lax.dynamic_slice_in_dim(tokens, me * width_part, width_part, 1)
    outgoing = select_rows(slot_list // 2, features)
    arrived = lax.all_to_all(outgoing, "dp", split_axis=0, concat_axis=0, tiled=True)

    slice_rows = gate_weight.shape[0]
    block_rows = slice_rows * tensor_count
    unit_cap = 2 * block_rows // owners
    unit_list, _ = place_rows(cluster_of[:, 0], owners, unit_cap)
    source = unit_list // slice_rows
    local = ((me - source) % tensor_count) * slice_rows + unit_list % slice_rows
    local = jnp.where(unit_list < block_rows, local, block_rows)

    gate_up = exchange_features(jnp.stack([gate_weight, up_weight]), tensor_count)
    arrived, gate_up = lax.optimization_barrier((arrived, gate_up))
    gate_own = lax.all_to_all(select_rows(local, gate_up[0]), "dp", split_axis=0, concat_axis=0, tiled=True)
    up_own = lax.all_to_all(select_rows(local, gate_up[1]), "dp", split_axis=0, concat_axis=0, tiled=True)
    down_rows = exchange_features(down_weight, tensor_count)
    gate_own, down_rows = lax.optimization_barrier((gate_own, down_rows))

    gate_part = against(arrived, gate_own).astype(jnp.bfloat16)
    gate_sum = lax.psum_scatter(gate_part, "tensor", scatter_dimension=0, tiled=True)
    gate_sum, up_own, down_rows = lax.optimization_barrier((gate_sum, up_own, down_rows))
    up_part = against(arrived, up_own).astype(jnp.bfloat16)
    down_own = lax.all_to_all(select_rows(local, down_rows), "dp", split_axis=0, concat_axis=0, tiled=True)
    up_sum = lax.psum_scatter(up_part, "tensor", scatter_dimension=0, tiled=True)
    gate_sum = gate_sum.astype(jnp.float32)
    hidden_part = (jax.nn.silu(gate_sum) * up_sum.astype(jnp.float32)).astype(jnp.bfloat16)
    hidden = lax.all_gather(hidden_part, "tensor", axis=0, tiled=True)
    expert_out = jnp.dot(hidden, down_own, preferred_element_type=jnp.float32).astype(jnp.bfloat16)
    returned = lax.all_to_all(expert_out, "dp", split_axis=0, concat_axis=0, tiled=True)

    spots = slot_spot.reshape(token_count, 2)
    columns = jnp.arange(returned.shape[0], dtype=jnp.int32)[None, :]
    weighting = (
        jnp.where(spots[:, 0:1] == columns, mixing[:, 0:1], 0.0)
        + jnp.where(spots[:, 1:2] == columns, mixing[:, 1:2], 0.0)
    )
    mixed_out = jnp.dot(
        weighting, returned.astype(jnp.float32), precision=lax.Precision.HIGHEST,
        preferred_element_type=jnp.float32,
    )
    return mixed_out.astype(jnp.bfloat16)


def solution(mesh):
    in_specs = (
        P("dp", None),
        P(),
        P(("dp", "tensor"), None),
        P(("dp", "tensor"), None),
        P(("dp", "tensor"), None),
        P("dp", None),
        P("dp", None),
    )
    out_specs = P("dp", "tensor")
    return jax.shard_map(
        on_device, mesh=mesh, in_specs=in_specs, out_specs=out_specs, check_vma=False
    )
```

```python
import jax
import jax.numpy as jnp
from jax import lax
from jax.sharding import PartitionSpec as P


def place_rows(labels, bin_count, capacity):
    count_rows = labels.shape[0]
    onehot = (labels[:, None] == jnp.arange(bin_count, dtype=jnp.int32)[None, :]).astype(jnp.int32)
    before = jnp.cumsum(onehot, axis=0) - onehot
    rank_in = jnp.sum(before * onehot, axis=1)
    position = labels * capacity + rank_in
    slot_list = jnp.full((bin_count * capacity,), count_rows, jnp.int32)
    slot_list = slot_list.at[position].set(jnp.arange(count_rows, dtype=jnp.int32))
    return (slot_list, position)


def against(left_side, right_side):
    return lax.dot_general(
        left_side, right_side, (((1,), (1,)), ((), ())), preferred_element_type=jnp.float32
    )


def select_rows(index, table):
    hot = (index[:, None] == jnp.arange(table.shape[0], dtype=jnp.int32)[None, :]).astype(table.dtype)
    return jnp.dot(hot, table, preferred_element_type=jnp.float32).astype(table.dtype)


def exchange_features(weights, tensor_count):
    me = lax.axis_index("tensor")
    lead = weights.shape[:-1]
    width = weights.shape[-1] // tensor_count
    blocks = weights.reshape(lead + (tensor_count, width))
    pieces = []
    for k in range(tensor_count):
        piece = lax.dynamic_index_in_dim(blocks, (me + k) % tensor_count, axis=len(lead), keepdims=False)
        if k:
            pairs = [(i, (i + k) % tensor_count) for i in range(tensor_count)]
            piece = lax.ppermute(piece, "tensor", pairs)
        pieces.append(piece)
    return jnp.concatenate(pieces, axis=len(lead) - 1)


def on_device(tokens, router_weight, gate_weight, up_weight, down_weight, cluster_of, expert_ids):
    owners = lax.axis_size("dp")
    tensor_count = lax.axis_size("tensor")
    width_part = tokens.shape[1] // tensor_count
    token_count = tokens.shape[0]
    me = lax.axis_index("tensor")

    logits = jnp.dot(tokens, router_weight, preferred_element_type=jnp.float32)
    scores = jax.nn.sigmoid(jnp.take_along_axis(logits, expert_ids, axis=1))
    mixing = scores / jnp.sum(scores, axis=1, keepdims=True)

    capacity = 4 * token_count // owners
    flat_ids = expert_ids.reshape(-1)
    slot_list, slot_spot = place_rows(flat_ids, owners, capacity)
    features = lax.dynamic_slice_in_dim(tokens, me * width_part, width_part, 1)
    outgoing = select_rows(slot_list // 2, features)
    arrived = lax.all_to_all(outgoing, "dp", split_axis=0, concat_axis=0, tiled=True)

    slice_rows = gate_weight.shape[0]
    block_rows = slice_rows * tensor_count
    unit_cap = 2 * block_rows // owners
    unit_list, _ = place_rows(cluster_of[:, 0], owners, unit_cap)
    source = unit_list // slice_rows
    local = ((me - source) % tensor_count) * slice_rows + unit_list % slice_rows
    local = jnp.where(unit_list < block_rows, local, block_rows)

    gate_rows = exchange_features(gate_weight, tensor_count)
    arrived, gate_rows = lax.optimization_barrier((arrived, gate_rows))
    gate_own = lax.all_to_all(select_rows(local, gate_rows), "dp", split_axis=0, concat_axis=0, tiled=True)
    up_rows = exchange_features(up_weight, tensor_count)
    down_rows = exchange_features(down_weight, tensor_count)
    gate_own, up_rows = lax.optimization_barrier((gate_own, up_rows))
    up_own = lax.all_to_all(select_rows(local, up_rows), "dp", split_axis=0, concat_axis=0, tiled=True)

    gate_part = against(arrived, gate_own).astype(jnp.bfloat16)
    gate_sum = lax.psum_scatter(gate_part, "tensor", scatter_dimension=0, tiled=True)
    gate_sum, up_own, down_rows = lax.optimization_barrier((gate_sum, up_own, down_rows))
    up_part = against(arrived, up_own).astype(jnp.bfloat16)
    down_own = lax.all_to_all(select_rows(local, down_rows), "dp", split_axis=0, concat_axis=0, tiled=True)
    up_sum = lax.psum_scatter(up_part, "tensor", scatter_dimension=0, tiled=True)
    gate_sum = gate_sum.astype(jnp.float32)
    hidden_part = (jax.nn.silu(gate_sum) * up_sum.astype(jnp.float32)).astype(jnp.bfloat16)
    hidden = lax.all_gather(hidden_part, "tensor", axis=0, tiled=True)
    expert_out = jnp.dot(hidden, down_own, preferred_element_type=jnp.float32).astype(jnp.bfloat16)
    returned = lax.all_to_all(expert_out, "dp", split_axis=0, concat_axis=0, tiled=True)

    spots = slot_spot.reshape(token_count, 2)
    columns = jnp.arange(returned.shape[0], dtype=jnp.int32)[None, :]
    weighting = (
        jnp.where(spots[:, 0:1] == columns, mixing[:, 0:1], 0.0)
        + jnp.where(spots[:, 1:2] == columns, mixing[:, 1:2], 0.0)
    )
    mixed_out = jnp.dot(
        weighting, returned.astype(jnp.float32), precision=lax.Precision.HIGHEST,
        preferred_element_type=jnp.float32,
    )
    return mixed_out.astype(jnp.bfloat16)


def solution(mesh):
    in_specs = (
        P("dp", None),
        P(),
        P(("dp", "tensor"), None),
        P(("dp", "tensor"), None),
        P(("dp", "tensor"), None),
        P("dp", None),
        P("dp", None),
    )
    out_specs = P("dp", "tensor")
    return jax.shard_map(
        on_device, mesh=mesh, in_specs=in_specs, out_specs=out_specs, check_vma=False
    )
```

```python
import jax
import jax.numpy as jnp
from jax import lax
from jax.sharding import PartitionSpec as P


def place_rows(labels, bin_count, capacity):
    count_rows = labels.shape[0]
    onehot = (labels[:, None] == jnp.arange(bin_count, dtype=jnp.int32)[None, :]).astype(jnp.int32)
    before = jnp.cumsum(onehot, axis=0) - onehot
    rank_in = jnp.sum(before * onehot, axis=1)
    position = labels * capacity + rank_in
    slot_list = jnp.full((bin_count * capacity,), count_rows, jnp.int32)
    slot_list = slot_list.at[position].set(jnp.arange(count_rows, dtype=jnp.int32))
    return (slot_list, position)


def against(left_side, right_side):
    return lax.dot_general(
        left_side, right_side, (((1,), (1,)), ((), ())), preferred_element_type=jnp.float32
    )


def select_rows(index, table):
    hot = (index[:, None] == jnp.arange(table.shape[0], dtype=jnp.int32)[None, :]).astype(table.dtype)
    return jnp.dot(hot, table, preferred_element_type=jnp.float32).astype(table.dtype)


def exchange_features(weights, tensor_count):
    me = lax.axis_index("tensor")
    lead = weights.shape[:-1]
    width = weights.shape[-1] // tensor_count
    blocks = weights.reshape(lead + (tensor_count, width))
    pieces = []
    for k in range(tensor_count):
        piece = lax.dynamic_index_in_dim(blocks, (me + k) % tensor_count, axis=len(lead), keepdims=False)
        if k:
            pairs = [(i, (i + k) % tensor_count) for i in range(tensor_count)]
            piece = lax.ppermute(piece, "tensor", pairs)
        pieces.append(piece)
    return jnp.concatenate(pieces, axis=len(lead) - 1)


def on_device(tokens, router_weight, gate_weight, up_weight, down_weight, cluster_of, expert_ids):
    owners = lax.axis_size("dp")
    tensor_count = lax.axis_size("tensor")
    width_part = tokens.shape[1] // tensor_count
    token_count = tokens.shape[0]
    me = lax.axis_index("tensor")

    logits = jnp.dot(tokens, router_weight, preferred_element_type=jnp.float32)
    scores = jax.nn.sigmoid(jnp.take_along_axis(logits, expert_ids, axis=1))
    mixing = scores / jnp.sum(scores, axis=1, keepdims=True)

    capacity = 4 * token_count // owners
    flat_ids = expert_ids.reshape(-1)
    slot_list, slot_spot = place_rows(flat_ids, owners, capacity)
    features = lax.dynamic_slice_in_dim(tokens, me * width_part, width_part, 1)
    outgoing = select_rows(slot_list // 2, features)
    arrived = lax.all_to_all(outgoing, "dp", split_axis=0, concat_axis=0, tiled=True)

    slice_rows = gate_weight.shape[0]
    block_rows = slice_rows * tensor_count
    unit_cap = 2 * block_rows // owners
    unit_list, _ = place_rows(cluster_of[:, 0], owners, unit_cap)
    source = unit_list // slice_rows
    local = ((me - source) % tensor_count) * slice_rows + unit_list % slice_rows
    local = jnp.where(unit_list < block_rows, local, block_rows)

    gate_up = exchange_features(jnp.stack([gate_weight, up_weight]), tensor_count)
    arrived, gate_up = lax.optimization_barrier((arrived, gate_up))
    gate_own = lax.all_to_all(select_rows(local, gate_up[0]), "dp", split_axis=0, concat_axis=0, tiled=True)
    up_own = lax.all_to_all(select_rows(local, gate_up[1]), "dp", split_axis=0, concat_axis=0, tiled=True)
    down_rows = exchange_features(down_weight, tensor_count)
    gate_own, down_rows = lax.optimization_barrier((gate_own, down_rows))

    groups = tensor_count
    per_group = owners // groups
    half = capacity // 2
    arrived = arrived.reshape(groups, per_group, 2, half, width_part).transpose(0, 2, 1, 3, 4)
    arrived = arrived.reshape(owners * capacity, width_part)

    gate_part = against(arrived, gate_own).astype(jnp.bfloat16)
    gate_sum = lax.psum_scatter(gate_part, "tensor", scatter_dimension=0, tiled=True)
    gate_sum, up_own, down_rows = lax.optimization_barrier((gate_sum, up_own, down_rows))
    up_part = against(arrived, up_own).astype(jnp.bfloat16)
    down_own = lax.all_to_all(select_rows(local, down_rows), "dp", split_axis=0, concat_axis=0, tiled=True)
    up_sum = lax.psum_scatter(up_part, "tensor", scatter_dimension=0, tiled=True)
    gate_sum = gate_sum.astype(jnp.float32)
    hidden_part = (jax.nn.silu(gate_sum) * up_sum.astype(jnp.float32)).astype(jnp.bfloat16)
    rows_half = hidden_part.shape[0] // 2

    spots = slot_spot.reshape(token_count, 2)
    columns = jnp.arange(owners * capacity, dtype=jnp.int32)[None, :]
    weighting = (
        jnp.where(spots[:, 0:1] == columns, mixing[:, 0:1], 0.0)
        + jnp.where(spots[:, 1:2] == columns, mixing[:, 1:2], 0.0)
    ).reshape(token_count, owners, 2, half)

    hidden_a = lax.all_gather(hidden_part[:rows_half], "tensor", axis=0, tiled=True)
    hidden_a, part_b = lax.optimization_barrier((hidden_a, hidden_part[rows_half:]))
    out_a = jnp.dot(hidden_a, down_own, preferred_element_type=jnp.float32).astype(jnp.bfloat16)
    returned_a = lax.all_to_all(out_a, "dp", split_axis=0, concat_axis=0, tiled=True)
    hidden_b = lax.all_gather(part_b, "tensor", axis=0, tiled=True)
    returned_a, hidden_b = lax.optimization_barrier((returned_a, hidden_b))
    out_b = jnp.dot(hidden_b, down_own, preferred_element_type=jnp.float32).astype(jnp.bfloat16)
    returned_b = lax.all_to_all(out_b, "dp", split_axis=0, concat_axis=0, tiled=True)

    mixed_out = jnp.dot(
        weighting[:, :, 0, :].reshape(token_count, owners * half), returned_a.astype(jnp.float32),
        precision=lax.Precision.HIGHEST, preferred_element_type=jnp.float32,
    ) + jnp.dot(
        weighting[:, :, 1, :].reshape(token_count, owners * half), returned_b.astype(jnp.float32),
        precision=lax.Precision.HIGHEST, preferred_element_type=jnp.float32,
    )
    return mixed_out.astype(jnp.bfloat16)


def solution(mesh):
    in_specs = (
        P("dp", None),
        P(),
        P(("dp", "tensor"), None),
        P(("dp", "tensor"), None),
        P(("dp", "tensor"), None),
        P("dp", None),
        P("dp", None),
    )
    out_specs = P("dp", "tensor")
    return jax.shard_map(
        on_device, mesh=mesh, in_specs=in_specs, out_specs=out_specs, check_vma=False
    )
```

```python
import jax
import jax.numpy as jnp
from jax import lax
from jax.sharding import PartitionSpec as P


def place_rows(labels, bin_count, capacity):
    count_rows = labels.shape[0]
    onehot = (labels[:, None] == jnp.arange(bin_count, dtype=jnp.int32)[None, :]).astype(jnp.int32)
    before = jnp.cumsum(onehot, axis=0) - onehot
    rank_in = jnp.sum(before * onehot, axis=1)
    position = labels * capacity + rank_in
    slot_list = jnp.full((bin_count * capacity,), count_rows, jnp.int32)
    slot_list = slot_list.at[position].set(jnp.arange(count_rows, dtype=jnp.int32))
    return (slot_list, position)


def against(left_side, right_side):
    return lax.dot_general(
        left_side, right_side, (((1,), (1,)), ((), ())), preferred_element_type=jnp.float32
    )


def select_rows(index, table):
    hot = (index[:, None] == jnp.arange(table.shape[0], dtype=jnp.int32)[None, :]).astype(table.dtype)
    return jnp.dot(hot, table, preferred_element_type=jnp.float32).astype(table.dtype)


def exchange_features(weights, tensor_count):
    me = lax.axis_index("tensor")
    lead = weights.shape[:-1]
    width = weights.shape[-1] // tensor_count
    blocks = weights.reshape(lead + (tensor_count, width))
    pieces = []
    for k in range(tensor_count):
        piece = lax.dynamic_index_in_dim(blocks, (me + k) % tensor_count, axis=len(lead), keepdims=False)
        if k:
            pairs = [(i, (i + k) % tensor_count) for i in range(tensor_count)]
            piece = lax.ppermute(piece, "tensor", pairs)
        pieces.append(piece)
    return jnp.concatenate(pieces, axis=len(lead) - 1)


def on_device(tokens, router_weight, gate_weight, up_weight, down_weight, cluster_of, expert_ids):
    owners = lax.axis_size("dp")
    tensor_count = lax.axis_size("tensor")
    width_part = tokens.shape[1] // tensor_count
    token_count = tokens.shape[0]
    me = lax.axis_index("tensor")

    logits = jnp.dot(tokens, router_weight, preferred_element_type=jnp.float32)
    scores = jax.nn.sigmoid(jnp.take_along_axis(logits, expert_ids, axis=1))
    mixing = scores / jnp.sum(scores, axis=1, keepdims=True)

    capacity = 4 * token_count // owners
    flat_ids = expert_ids.reshape(-1)
    slot_list, slot_spot = place_rows(flat_ids, owners, capacity)
    features = lax.dynamic_slice_in_dim(tokens, me * width_part, width_part, 1)
    outgoing = select_rows(slot_list // 2, features)
    arrived = lax.all_to_all(outgoing, "dp", split_axis=0, concat_axis=0, tiled=True)

    slice_rows = gate_weight.shape[0]
    block_rows = slice_rows * tensor_count
    unit_cap = 2 * block_rows // owners
    unit_list, _ = place_rows(cluster_of[:, 0], owners, unit_cap)
    source = unit_list // slice_rows
    local = ((me - source) % tensor_count) * slice_rows + unit_list % slice_rows
    local = jnp.where(unit_list < block_rows, local, block_rows)

    gate_up = exchange_features(jnp.stack([gate_weight, up_weight]), tensor_count)
    arrived, gate_up = lax.optimization_barrier((arrived, gate_up))
    hot = (local[:, None] == jnp.arange(block_rows, dtype=jnp.int32)[None, :]).astype(gate_up.dtype)
    pick = jnp.einsum("sn,wnf->wsf", hot, gate_up, preferred_element_type=jnp.float32).astype(gate_up.dtype)
    gate_up_own = lax.all_to_all(pick, "dp", split_axis=1, concat_axis=1, tiled=True)
    down_rows = exchange_features(down_weight, tensor_count)
    gate_up_own, down_rows = lax.optimization_barrier((gate_up_own, down_rows))

    gate_part = against(arrived, gate_up_own[0]).astype(jnp.bfloat16)
    up_part = against(arrived, gate_up_own[1]).astype(jnp.bfloat16)
    down_own = lax.all_to_all(select_rows(local, down_rows), "dp", split_axis=0, concat_axis=0, tiled=True)
    both = jnp.stack([gate_part, up_part], axis=1)
    summed = lax.psum_scatter(both, "tensor", scatter_dimension=0, tiled=True).astype(jnp.float32)
    hidden_part = (jax.nn.silu(summed[:, 0, :]) * summed[:, 1, :]).astype(jnp.bfloat16)
    hidden = lax.all_gather(hidden_part, "tensor", axis=0, tiled=True)
    expert_out = jnp.dot(hidden, down_own, preferred_element_type=jnp.float32).astype(jnp.bfloat16)
    returned = lax.all_to_all(expert_out, "dp", split_axis=0, concat_axis=0, tiled=True)

    spots = slot_spot.reshape(token_count, 2)
    columns = jnp.arange(returned.shape[0], dtype=jnp.int32)[None, :]
    weighting = (
        jnp.where(spots[:, 0:1] == columns, mixing[:, 0:1], 0.0)
        + jnp.where(spots[:, 1:2] == columns, mixing[:, 1:2], 0.0)
    )
    mixed_out = jnp.dot(
        weighting, returned.astype(jnp.float32), precision=lax.Precision.HIGHEST,
        preferred_element_type=jnp.float32,
    )
    return mixed_out.astype(jnp.bfloat16)


def solution(mesh):
    in_specs = (
        P("dp", None),
        P(),
        P(("dp", "tensor"), None),
        P(("dp", "tensor"), None),
        P(("dp", "tensor"), None),
        P("dp", None),
        P("dp", None),
    )
    out_specs = P("dp", "tensor")
    return jax.shard_map(
        on_device, mesh=mesh, in_specs=in_specs, out_specs=out_specs, check_vma=False
    )
```

```python
import jax
import jax.numpy as jnp
from jax import lax
from jax.sharding import PartitionSpec as P


def place_rows(labels, bin_count, capacity):
    count_rows = labels.shape[0]
    onehot = (labels[:, None] == jnp.arange(bin_count, dtype=jnp.int32)[None, :]).astype(jnp.int32)
    before = jnp.cumsum(onehot, axis=0) - onehot
    rank_in = jnp.sum(before * onehot, axis=1)
    position = labels * capacity + rank_in
    slot_list = jnp.full((bin_count * capacity,), count_rows, jnp.int32)
    slot_list = slot_list.at[position].set(jnp.arange(count_rows, dtype=jnp.int32))
    return (slot_list, position)


def against(left_side, right_side):
    return lax.dot_general(
        left_side, right_side, (((1,), (1,)), ((), ())), preferred_element_type=jnp.float32
    )


def select_rows(index, table):
    hot = (index[:, None] == jnp.arange(table.shape[0], dtype=jnp.int32)[None, :]).astype(table.dtype)
    return jnp.dot(hot, table, preferred_element_type=jnp.float32).astype(table.dtype)


def exchange_features(weights, tensor_count, row_axis):
    me = lax.axis_index("tensor")
    lead = weights.shape[:-1]
    width = weights.shape[-1] // tensor_count
    blocks = weights.reshape(lead + (tensor_count, width))
    pieces = []
    for k in range(tensor_count):
        piece = lax.dynamic_index_in_dim(blocks, (me + k) % tensor_count, axis=len(lead), keepdims=False)
        if k:
            pairs = [(i, (i + k) % tensor_count) for i in range(tensor_count)]
            piece = lax.ppermute(piece, "tensor", pairs)
        pieces.append(piece)
    return jnp.concatenate(pieces, axis=row_axis)


def on_device(tokens, router_weight, gate_weight, up_weight, down_weight, cluster_of, expert_ids):
    owners = lax.axis_size("dp")
    tensor_count = lax.axis_size("tensor")
    width_part = tokens.shape[1] // tensor_count
    token_count = tokens.shape[0]
    me = lax.axis_index("tensor")

    logits = jnp.dot(tokens, router_weight, preferred_element_type=jnp.float32)
    scores = jax.nn.sigmoid(jnp.take_along_axis(logits, expert_ids, axis=1))
    mixing = scores / jnp.sum(scores, axis=1, keepdims=True)

    capacity = 4 * token_count // owners
    flat_ids = expert_ids.reshape(-1)
    slot_list, slot_spot = place_rows(flat_ids, owners, capacity)
    features = lax.dynamic_slice_in_dim(tokens, me * width_part, width_part, 1)
    outgoing = select_rows(slot_list // 2, features)
    arrived = lax.all_to_all(outgoing, "dp", split_axis=0, concat_axis=0, tiled=True)

    slice_rows = gate_weight.shape[0]
    block_rows = slice_rows * tensor_count
    unit_cap = 2 * block_rows // owners
    unit_list, _ = place_rows(cluster_of[:, 0], owners, unit_cap)
    source = unit_list // slice_rows
    local = ((me - source) % tensor_count) * slice_rows + unit_list % slice_rows
    local = jnp.where(unit_list < block_rows, local, block_rows)

    gate_up = exchange_features(jnp.stack([gate_weight, up_weight], axis=1), tensor_count, 0)
    arrived, gate_up = lax.optimization_barrier((arrived, gate_up))
    pick = select_rows(local, gate_up.reshape(block_rows, 2 * width_part))
    gate_up_own = lax.all_to_all(pick, "dp", split_axis=0, concat_axis=0, tiled=True)
    down_rows = exchange_features(down_weight, tensor_count, 0)
    gate_up_own, down_rows = lax.optimization_barrier((gate_up_own, down_rows))

    gate_part = against(arrived, gate_up_own[:, :width_part]).astype(jnp.bfloat16)
    up_part = against(arrived, gate_up_own[:, width_part:]).astype(jnp.bfloat16)
    down_own = lax.all_to_all(select_rows(local, down_rows), "dp", split_axis=0, concat_axis=0, tiled=True)
    both = jnp.stack([gate_part, up_part], axis=1)
    summed = lax.psum_scatter(both, "tensor", scatter_dimension=0, tiled=True).astype(jnp.float32)
    hidden_part = (jax.nn.silu(summed[:, 0, :]) * summed[:, 1, :]).astype(jnp.bfloat16)
    hidden = lax.all_gather(hidden_part, "tensor", axis=0, tiled=True)
    expert_out = jnp.dot(hidden, down_own, preferred_element_type=jnp.float32).astype(jnp.bfloat16)
    returned = lax.all_to_all(expert_out, "dp", split_axis=0, concat_axis=0, tiled=True)

    spots = slot_spot.reshape(token_count, 2)
    columns = jnp.arange(returned.shape[0], dtype=jnp.int32)[None, :]
    weighting = (
        jnp.where(spots[:, 0:1] == columns, mixing[:, 0:1], 0.0)
        + jnp.where(spots[:, 1:2] == columns, mixing[:, 1:2], 0.0)
    )
    mixed_out = jnp.dot(
        weighting, returned.astype(jnp.float32), precision=lax.Precision.HIGHEST,
        preferred_element_type=jnp.float32,
    )
    return mixed_out.astype(jnp.bfloat16)


def solution(mesh):
    in_specs = (
        P("dp", None),
        P(),
        P(("dp", "tensor"), None),
        P(("dp", "tensor"), None),
        P(("dp", "tensor"), None),
        P("dp", None),
        P("dp", None),
    )
    out_specs = P("dp", "tensor")
    return jax.shard_map(
        on_device, mesh=mesh, in_specs=in_specs, out_specs=out_specs, check_vma=False
    )
```

```python
import jax
import jax.numpy as jnp
from jax import lax
from jax.sharding import PartitionSpec as P


def place_rows(labels, bin_count, capacity):
    count_rows = labels.shape[0]
    onehot = (labels[:, None] == jnp.arange(bin_count, dtype=jnp.int32)[None, :]).astype(jnp.int32)
    before = jnp.cumsum(onehot, axis=0) - onehot
    rank_in = jnp.sum(before * onehot, axis=1)
    position = labels * capacity + rank_in
    slot_list = jnp.full((bin_count * capacity,), count_rows, jnp.int32)
    slot_list = slot_list.at[position].set(jnp.arange(count_rows, dtype=jnp.int32))
    return (slot_list, position)


def against(left_side, right_side):
    return lax.dot_general(
        left_side, right_side, (((1,), (1,)), ((), ())), preferred_element_type=jnp.float32
    )


def select_rows(index, table):
    hot = (index[:, None] == jnp.arange(table.shape[0], dtype=jnp.int32)[None, :]).astype(table.dtype)
    return jnp.dot(hot, table, preferred_element_type=jnp.float32).astype(table.dtype)


def exchange_features(weights, tensor_count):
    me = lax.axis_index("tensor")
    lead = weights.shape[:-1]
    width = weights.shape[-1] // tensor_count
    blocks = weights.reshape(lead + (tensor_count, width))
    pieces = []
    for k in range(tensor_count):
        piece = lax.dynamic_index_in_dim(blocks, (me + k) % tensor_count, axis=len(lead), keepdims=False)
        if k:
            pairs = [(i, (i + k) % tensor_count) for i in range(tensor_count)]
            piece = lax.ppermute(piece, "tensor", pairs)
        pieces.append(piece)
    return jnp.concatenate(pieces, axis=len(lead) - 1)


def on_device(tokens, router_weight, gate_weight, up_weight, down_weight, cluster_of, expert_ids):
    owners = lax.axis_size("dp")
    tensor_count = lax.axis_size("tensor")
    width_part = tokens.shape[1] // tensor_count
    token_count = tokens.shape[0]
    me = lax.axis_index("tensor")

    logits = jnp.dot(tokens, router_weight, preferred_element_type=jnp.float32)
    scores = jax.nn.sigmoid(jnp.take_along_axis(logits, expert_ids, axis=1))
    mixing = scores / jnp.sum(scores, axis=1, keepdims=True)

    capacity = 4 * token_count // owners
    flat_ids = expert_ids.reshape(-1)
    slot_list, slot_spot = place_rows(flat_ids, owners, capacity)
    features = lax.dynamic_slice_in_dim(tokens, me * width_part, width_part, 1)
    outgoing = select_rows(slot_list // 2, features)
    arrived = lax.all_to_all(outgoing, "dp", split_axis=0, concat_axis=0, tiled=True)

    slice_rows = gate_weight.shape[0]
    block_rows = slice_rows * tensor_count
    unit_cap = 2 * block_rows // owners
    unit_list, _ = place_rows(cluster_of[:, 0], owners, unit_cap)
    source = unit_list // slice_rows
    local = ((me - source) % tensor_count) * slice_rows + unit_list % slice_rows
    local = jnp.where(unit_list < block_rows, local, block_rows)

    gate_up = exchange_features(jnp.stack([gate_weight, up_weight]), tensor_count)
    arrived, gate_up = lax.optimization_barrier((arrived, gate_up))
    hot = (local[:, None] == jnp.arange(block_rows, dtype=jnp.int32)[None, :]).astype(gate_up.dtype)
    pick = jnp.einsum("sn,wnf->wsf", hot, gate_up, preferred_element_type=jnp.float32).astype(gate_up.dtype)
    gate_up_own = lax.all_to_all(pick, "dp", split_axis=1, concat_axis=1, tiled=True)
    down_rows = exchange_features(down_weight, tensor_count)
    gate_up_own, down_rows = lax.optimization_barrier((gate_up_own, down_rows))

    gate_part = against(arrived, gate_up_own[0]).astype(jnp.bfloat16)
    up_part = against(arrived, gate_up_own[1]).astype(jnp.bfloat16)
    down_own = lax.all_to_all(select_rows(local, down_rows), "dp", split_axis=0, concat_axis=0, tiled=True)
    both = jnp.stack([gate_part, up_part], axis=1)
    summed = lax.psum(both, "tensor").astype(jnp.float32)
    hidden = (jax.nn.silu(summed[:, 0, :]) * summed[:, 1, :]).astype(jnp.bfloat16)
    expert_out = jnp.dot(hidden, down_own, preferred_element_type=jnp.float32).astype(jnp.bfloat16)
    returned = lax.all_to_all(expert_out, "dp", split_axis=0, concat_axis=0, tiled=True)

    spots = slot_spot.reshape(token_count, 2)
    columns = jnp.arange(returned.shape[0], dtype=jnp.int32)[None, :]
    weighting = (
        jnp.where(spots[:, 0:1] == columns, mixing[:, 0:1], 0.0)
        + jnp.where(spots[:, 1:2] == columns, mixing[:, 1:2], 0.0)
    )
    mixed_out = jnp.dot(
        weighting, returned.astype(jnp.float32), precision=lax.Precision.HIGHEST,
        preferred_element_type=jnp.float32,
    )
    return mixed_out.astype(jnp.bfloat16)


def solution(mesh):
    in_specs = (
        P("dp", None),
        P(),
        P(("dp", "tensor"), None),
        P(("dp", "tensor"), None),
        P(("dp", "tensor"), None),
        P("dp", None),
        P("dp", None),
    )
    out_specs = P("dp", "tensor")
    return jax.shard_map(
        on_device, mesh=mesh, in_specs=in_specs, out_specs=out_specs, check_vma=False
    )
```

```python
import jax
import jax.numpy as jnp
from jax import lax
from jax.sharding import PartitionSpec as P


def place_rows(labels, bin_count, capacity):
    count_rows = labels.shape[0]
    onehot = (labels[:, None] == jnp.arange(bin_count, dtype=jnp.int32)[None, :]).astype(jnp.int32)
    before = jnp.cumsum(onehot, axis=0) - onehot
    rank_in = jnp.sum(before * onehot, axis=1)
    position = labels * capacity + rank_in
    slot_list = jnp.full((bin_count * capacity,), count_rows, jnp.int32)
    slot_list = slot_list.at[position].set(jnp.arange(count_rows, dtype=jnp.int32))
    return (slot_list, position)


def against(left_side, right_side):
    return lax.dot_general(
        left_side, right_side, (((1,), (1,)), ((), ())), preferred_element_type=jnp.float32
    )


def select_rows(index, table):
    hot = (index[:, None] == jnp.arange(table.shape[0], dtype=jnp.int32)[None, :]).astype(table.dtype)
    return jnp.dot(hot, table, preferred_element_type=jnp.float32).astype(table.dtype)


def exchange_features(weights, tensor_count):
    me = lax.axis_index("tensor")
    lead = weights.shape[:-1]
    width = weights.shape[-1] // tensor_count
    blocks = weights.reshape(lead + (tensor_count, width))
    pieces = []
    for k in range(tensor_count):
        piece = lax.dynamic_index_in_dim(blocks, (me + k) % tensor_count, axis=len(lead), keepdims=False)
        if k:
            pairs = [(i, (i + k) % tensor_count) for i in range(tensor_count)]
            piece = lax.ppermute(piece, "tensor", pairs)
        pieces.append(piece)
    return jnp.concatenate(pieces, axis=len(lead) - 1)


def on_device(tokens, router_weight, gate_weight, up_weight, down_weight, cluster_of, expert_ids):
    owners = lax.axis_size("dp")
    tensor_count = lax.axis_size("tensor")
    width_part = tokens.shape[1] // tensor_count
    token_count = tokens.shape[0]
    me = lax.axis_index("tensor")

    logits = jnp.dot(tokens, router_weight, preferred_element_type=jnp.float32)
    scores = jax.nn.sigmoid(jnp.take_along_axis(logits, expert_ids, axis=1))
    mixing = scores / jnp.sum(scores, axis=1, keepdims=True)

    capacity = 4 * token_count // owners
    flat_ids = expert_ids.reshape(-1)
    slot_list, slot_spot = place_rows(flat_ids, owners, capacity)
    features = lax.dynamic_slice_in_dim(tokens, me * width_part, width_part, 1)
    outgoing = select_rows(slot_list // 2, features)
    arrived = lax.all_to_all(outgoing, "dp", split_axis=0, concat_axis=0, tiled=True)

    slice_rows = gate_weight.shape[0]
    block_rows = slice_rows * tensor_count
    unit_cap = 2 * block_rows // owners
    unit_list, _ = place_rows(cluster_of[:, 0], owners, unit_cap)
    source = unit_list // slice_rows
    local = ((me - source) % tensor_count) * slice_rows + unit_list % slice_rows
    local = jnp.where(unit_list < block_rows, local, block_rows)

    gate_up = exchange_features(jnp.stack([gate_weight, up_weight]), tensor_count)
    arrived, gate_up = lax.optimization_barrier((arrived, gate_up))
    hot = (local[:, None] == jnp.arange(block_rows, dtype=jnp.int32)[None, :]).astype(gate_up.dtype)
    pick = jnp.einsum("sn,wnf->wsf", hot, gate_up, preferred_element_type=jnp.float32).astype(gate_up.dtype)
    gate_up_own = lax.all_to_all(pick, "dp", split_axis=1, concat_axis=1, tiled=True)
    down_rows = lax.all_to_all(down_weight, "tensor", split_axis=1, concat_axis=0, tiled=True)
    natural = jnp.where(unit_list < block_rows, unit_list, block_rows)

    gate_part = against(arrived, gate_up_own[0]).astype(jnp.bfloat16)
    up_part = against(arrived, gate_up_own[1]).astype(jnp.bfloat16)
    down_own = lax.all_to_all(select_rows(natural, down_rows), "dp", split_axis=0, concat_axis=0, tiled=True)
    both = jnp.stack([gate_part, up_part], axis=1)
    summed = lax.psum(both, "tensor").astype(jnp.float32)
    hidden = (jax.nn.silu(summed[:, 0, :]) * summed[:, 1, :]).astype(jnp.bfloat16)
    expert_out = jnp.dot(hidden, down_own, preferred_element_type=jnp.float32).astype(jnp.bfloat16)
    returned = lax.all_to_all(expert_out, "dp", split_axis=0, concat_axis=0, tiled=True)

    spots = slot_spot.reshape(token_count, 2)
    columns = jnp.arange(returned.shape[0], dtype=jnp.int32)[None, :]
    weighting = (
        jnp.where(spots[:, 0:1] == columns, mixing[:, 0:1], 0.0)
        + jnp.where(spots[:, 1:2] == columns, mixing[:, 1:2], 0.0)
    )
    mixed_out = jnp.dot(
        weighting, returned.astype(jnp.float32), precision=lax.Precision.HIGHEST,
        preferred_element_type=jnp.float32,
    )
    return mixed_out.astype(jnp.bfloat16)


def solution(mesh):
    in_specs = (
        P("dp", None),
        P(),
        P(("dp", "tensor"), None),
        P(("dp", "tensor"), None),
        P(("dp", "tensor"), None),
        P("dp", None),
        P("dp", None),
    )
    out_specs = P("dp", "tensor")
    return jax.shard_map(
        on_device, mesh=mesh, in_specs=in_specs, out_specs=out_specs, check_vma=False
    )
```

```python
import jax
import jax.numpy as jnp
from jax import lax
from jax.sharding import PartitionSpec as P


def place_rows(labels, bin_count, capacity):
    count_rows = labels.shape[0]
    onehot = (labels[:, None] == jnp.arange(bin_count, dtype=jnp.int32)[None, :]).astype(jnp.int32)
    before = jnp.cumsum(onehot, axis=0) - onehot
    rank_in = jnp.sum(before * onehot, axis=1)
    position = labels * capacity + rank_in
    slot_list = jnp.full((bin_count * capacity,), count_rows, jnp.int32)
    slot_list = slot_list.at[position].set(jnp.arange(count_rows, dtype=jnp.int32))
    return (slot_list, position)


def against(left_side, right_side):
    return lax.dot_general(
        left_side, right_side, (((1,), (1,)), ((), ())), preferred_element_type=jnp.float32
    )


def select_rows(index, table):
    hot = (index[:, None] == jnp.arange(table.shape[0], dtype=jnp.int32)[None, :]).astype(table.dtype)
    return jnp.dot(hot, table, preferred_element_type=jnp.float32).astype(table.dtype)


def exchange_features(weights, tensor_count):
    me = lax.axis_index("tensor")
    lead = weights.shape[:-1]
    width = weights.shape[-1] // tensor_count
    blocks = weights.reshape(lead + (tensor_count, width))
    pieces = []
    for k in range(tensor_count):
        piece = lax.dynamic_index_in_dim(blocks, (me + k) % tensor_count, axis=len(lead), keepdims=False)
        if k:
            pairs = [(i, (i + k) % tensor_count) for i in range(tensor_count)]
            piece = lax.ppermute(piece, "tensor", pairs)
        pieces.append(piece)
    return jnp.concatenate(pieces, axis=len(lead) - 1)


def on_device(tokens, router_weight, gate_weight, up_weight, down_weight, cluster_of, expert_ids):
    owners = lax.axis_size("dp")
    tensor_count = lax.axis_size("tensor")
    width_part = tokens.shape[1] // tensor_count
    token_count = tokens.shape[0]
    me = lax.axis_index("tensor")

    logits = jnp.dot(tokens, router_weight, preferred_element_type=jnp.float32)
    scores = jax.nn.sigmoid(jnp.take_along_axis(logits, expert_ids, axis=1))
    mixing = scores / jnp.sum(scores, axis=1, keepdims=True)

    capacity = 4 * token_count // owners
    flat_ids = expert_ids.reshape(-1)
    slot_list, slot_spot = place_rows(flat_ids, owners, capacity)
    features = lax.dynamic_slice_in_dim(tokens, me * width_part, width_part, 1)
    outgoing = select_rows(slot_list // 2, features)
    arrived = lax.all_to_all(outgoing, "dp", split_axis=0, concat_axis=0, tiled=True)

    slice_rows = gate_weight.shape[0]
    block_rows = slice_rows * tensor_count
    unit_cap = -(-(2 * block_rows // owners) // 8) * 8
    unit_list, _ = place_rows(cluster_of[:, 0], owners, unit_cap)
    source = unit_list // slice_rows
    local = ((me - source) % tensor_count) * slice_rows + unit_list % slice_rows
    local = jnp.where(unit_list < block_rows, local, block_rows)

    gate_up = exchange_features(jnp.stack([gate_weight, up_weight]), tensor_count)
    arrived, gate_up = lax.optimization_barrier((arrived, gate_up))
    hot = (local[:, None] == jnp.arange(block_rows, dtype=jnp.int32)[None, :]).astype(gate_up.dtype)
    pick = jnp.einsum("sn,wnf->wsf", hot, gate_up, preferred_element_type=jnp.float32).astype(gate_up.dtype)
    gate_up_own = lax.all_to_all(pick, "dp", split_axis=1, concat_axis=1, tiled=True)
    down_rows = exchange_features(down_weight, tensor_count)
    gate_up_own, down_rows = lax.optimization_barrier((gate_up_own, down_rows))

    gate_part = against(arrived, gate_up_own[0]).astype(jnp.bfloat16)
    up_part = against(arrived, gate_up_own[1]).astype(jnp.bfloat16)
    down_own = lax.all_to_all(select_rows(local, down_rows), "dp", split_axis=0, concat_axis=0, tiled=True)
    both = jnp.stack([gate_part, up_part], axis=1)
    summed = lax.psum(both, "tensor").astype(jnp.float32)
    hidden = (jax.nn.silu(summed[:, 0, :]) * summed[:, 1, :]).astype(jnp.bfloat16)
    expert_out = jnp.dot(hidden, down_own, preferred_element_type=jnp.float32).astype(jnp.bfloat16)
    returned = lax.all_to_all(expert_out, "dp", split_axis=0, concat_axis=0, tiled=True)

    spots = slot_spot.reshape(token_count, 2)
    columns = jnp.arange(returned.shape[0], dtype=jnp.int32)[None, :]
    weighting = (
        jnp.where(spots[:, 0:1] == columns, mixing[:, 0:1], 0.0)
        + jnp.where(spots[:, 1:2] == columns, mixing[:, 1:2], 0.0)
    )
    mixed_out = jnp.dot(
        weighting, returned.astype(jnp.float32), precision=lax.Precision.HIGHEST,
        preferred_element_type=jnp.float32,
    )
    return mixed_out.astype(jnp.bfloat16)


def solution(mesh):
    in_specs = (
        P("dp", None),
        P(),
        P(("dp", "tensor"), None),
        P(("dp", "tensor"), None),
        P(("dp", "tensor"), None),
        P("dp", None),
        P("dp", None),
    )
    out_specs = P("dp", "tensor")
    return jax.shard_map(
        on_device, mesh=mesh, in_specs=in_specs, out_specs=out_specs, check_vma=False
    )
```

```python
import jax
import jax.numpy as jnp
from jax import lax
from jax.sharding import PartitionSpec as P


def place_rows(labels, bin_count, capacity):
    count_rows = labels.shape[0]
    onehot = (labels[:, None] == jnp.arange(bin_count, dtype=jnp.int32)[None, :]).astype(jnp.int32)
    before = jnp.cumsum(onehot, axis=0) - onehot
    rank_in = jnp.sum(before * onehot, axis=1)
    position = labels * capacity + rank_in
    slot_list = jnp.full((bin_count * capacity,), count_rows, jnp.int32)
    slot_list = slot_list.at[position].set(jnp.arange(count_rows, dtype=jnp.int32))
    return (slot_list, position)


def against(left_side, right_side):
    return lax.dot_general(
        left_side, right_side, (((1,), (1,)), ((), ())), preferred_element_type=jnp.float32
    )


def select_rows(index, table):
    hot = (index[:, None] == jnp.arange(table.shape[0], dtype=jnp.int32)[None, :]).astype(table.dtype)
    return jnp.dot(hot, table, preferred_element_type=jnp.float32).astype(table.dtype)


def exchange_features(weights, tensor_count):
    me = lax.axis_index("tensor")
    lead = weights.shape[:-1]
    width = weights.shape[-1] // tensor_count
    blocks = weights.reshape(lead + (tensor_count, width))
    pieces = []
    for k in range(tensor_count):
        piece = lax.dynamic_index_in_dim(blocks, (me + k) % tensor_count, axis=len(lead), keepdims=False)
        if k:
            pairs = [(i, (i + k) % tensor_count) for i in range(tensor_count)]
            piece = lax.ppermute(piece, "tensor", pairs)
        pieces.append(piece)
    return jnp.concatenate(pieces, axis=len(lead) - 1)


def on_device(tokens, router_weight, gate_weight, up_weight, down_weight, cluster_of, expert_ids):
    owners = lax.axis_size("dp")
    tensor_count = lax.axis_size("tensor")
    width_part = tokens.shape[1] // tensor_count
    token_count = tokens.shape[0]
    me = lax.axis_index("tensor")

    logits = jnp.dot(tokens, router_weight, preferred_element_type=jnp.float32)
    scores = jax.nn.sigmoid(jnp.take_along_axis(logits, expert_ids, axis=1))
    mixing = scores / jnp.sum(scores, axis=1, keepdims=True)

    capacity = 4 * token_count // owners
    flat_ids = expert_ids.reshape(-1)
    slot_list, slot_spot = place_rows(flat_ids, owners, capacity)
    features = lax.dynamic_slice_in_dim(tokens, me * width_part, width_part, 1)
    outgoing = select_rows(slot_list // 2, features)
    arrived = lax.all_to_all(outgoing, "dp", split_axis=0, concat_axis=0, tiled=True)

    slice_rows = gate_weight.shape[0]
    block_rows = slice_rows * tensor_count
    unit_cap = 2 * block_rows // owners
    unit_list, _ = place_rows(cluster_of[:, 0], owners, unit_cap)
    source = unit_list // slice_rows
    local = ((me - source) % tensor_count) * slice_rows + unit_list % slice_rows
    local = jnp.where(unit_list < block_rows, local, block_rows)

    gate_up = exchange_features(jnp.stack([gate_weight, up_weight]), tensor_count)
    arrived, gate_up = lax.optimization_barrier((arrived, gate_up))
    hot = (local[:, None] == jnp.arange(block_rows, dtype=jnp.int32)[None, :]).astype(gate_up.dtype)
    pick = jnp.einsum("sn,wnf->wsf", hot, gate_up, preferred_element_type=jnp.float32).astype(gate_up.dtype)
    gate_up_own = lax.all_to_all(pick, "dp", split_axis=1, concat_axis=1, tiled=True)
    down_rows = exchange_features(down_weight, tensor_count)
    gate_up_own, down_rows = lax.optimization_barrier((gate_up_own, down_rows))

    stacked_own = gate_up_own.reshape(2 * gate_up_own.shape[1], width_part)
    both = against(arrived, stacked_own).astype(jnp.bfloat16).reshape(arrived.shape[0], 2, gate_up_own.shape[1])
    down_own = lax.all_to_all(select_rows(local, down_rows), "dp", split_axis=0, concat_axis=0, tiled=True)
    summed = lax.psum(both, "tensor").astype(jnp.float32)
    hidden = (jax.nn.silu(summed[:, 0, :]) * summed[:, 1, :]).astype(jnp.bfloat16)
    expert_out = jnp.dot(hidden, down_own, preferred_element_type=jnp.float32).astype(jnp.bfloat16)
    returned = lax.all_to_all(expert_out, "dp", split_axis=0, concat_axis=0, tiled=True)

    spots = slot_spot.reshape(token_count, 2)
    columns = jnp.arange(returned.shape[0], dtype=jnp.int32)[None, :]
    weighting = (
        jnp.where(spots[:, 0:1] == columns, mixing[:, 0:1], 0.0)
        + jnp.where(spots[:, 1:2] == columns, mixing[:, 1:2], 0.0)
    )
    mixed_out = jnp.dot(
        weighting, returned.astype(jnp.float32), precision=lax.Precision.HIGHEST,
        preferred_element_type=jnp.float32,
    )
    return mixed_out.astype(jnp.bfloat16)


def solution(mesh):
    in_specs = (
        P("dp", None),
        P(),
        P(("dp", "tensor"), None),
        P(("dp", "tensor"), None),
        P(("dp", "tensor"), None),
        P("dp", None),
        P("dp", None),
    )
    out_specs = P("dp", "tensor")
    return jax.shard_map(
        on_device, mesh=mesh, in_specs=in_specs, out_specs=out_specs, check_vma=False
    )
```
